512 devices in a mesh: req: 64 (over x, z, core), ch: 8 (over y).
Axes of the slice: x: 4, y: 8, z: 8, core: 2. Of those that a mesh axis runs over, the one named last changes fastest.
Arguments:
- tokens: bfloat16 [128, 4096], P('req', 'ch'), may hold values from -80 to 80
- attn_gain: float32 [4096], P('ch'), may hold values from 0.1 to 1.9
- w_query: bfloat16 [4096, 4096], P('ch', 'req'), may hold values from -0.09375 to 0.09375
- w_keyval: bfloat16 [4096, 512], P('ch', 'req'), may hold values from -0.09375 to 0.09375
- cache: bfloat16 [2, 128, 256, 2048], P(None, 'req', 'ch'), may hold values from -70 to 70
- lengths: int32 [128], P('req'), may hold values from 1 to 2047, as said below
- write_pos: int32 [128], P('req'), may hold values from 0 to 2047
- w_out: bfloat16 [4096, 4096], P('ch', 'req'), may hold values from -0.09375 to 0.09375
- mlp_gain: float32 [4096], P('ch'), may hold values from 0.1 to 1.9
- w_gate_up: bfloat16 [4096, 24576], P('ch', 'req'), may hold values from -0.09375 to 0.09375
- w_down: bfloat16 [12288, 4096], P('req', 'ch'), may hold values from -0.0546875 to 0.0546875
Outputs:
- layer_out: bfloat16 [128, 4096], P('req', 'ch')
- kv_new: bfloat16 [128, 512], P('req', 'ch')
The draws below stay inside these ranges and needn't reach their ends.
Inputs may be any that keep to these rules, and one draw needn't show every extreme that they name: lengths[b] earlier tokens of request b are in the cache; the largest equals 2047 in every draw. The new token of request b goes to slot write_pos[b]; its earlier tokens fill the slots before it, going back cyclically.
All inputs are finite; a program needn't handle non-finite values.
Results may differ from the reference program's by a relative error of at most 0.0064.
Values may be sent and summed in bfloat16 or wider, within the bound.
No kernel may reach another device: no remote copies, remote signals or barrier semaphores. Data moves between devices by JAX's collectives and lax.ppermute only.
A program may use at most 64 MiB of HBM per device.

```python
import math
import jax
import jax.numpy as jnp
from jax import lax

D = 4096
FF = 12288
H = 16
HD = 256
WINDOW = 2048
TOKENS = 128
N_REQ = 64
N_CH = 8


def draw_tokens(key, part):
    first_key = jax.random.fold_in(jax.random.fold_in(key, 11), 0)
    ramp = jnp.exp(math.log(3.0) * jnp.arange(D, dtype=jnp.float32) / D)
    base = jnp.clip(jax.random.normal(first_key, (TOKENS, D), jnp.float32), -6.0, 6.0)
    return (base * ramp[None, :]).astype(jnp.bfloat16)


def draw_cache(key, part):
    first_key = jax.random.fold_in(jax.random.fold_in(key, 23), 0)
    base = jnp.clip(jax.random.normal(first_key, (2, TOKENS, HD, WINDOW), jnp.float32), -6.0, 6.0)
    return base.astype(jnp.bfloat16)


def draw_lengths(key, part):
    first_key, second_key = jax.random.split(jax.random.fold_in(key, 37))
    uniform_int = jax.random.randint(first_key, (TOKENS,), 0, WINDOW, dtype=jnp.int32)
    cubed = uniform_int * uniform_int // WINDOW * uniform_int // WINDOW
    counts = 1 + cubed
    chosen = jax.random.randint(second_key, (), 0, TOKENS, dtype=jnp.int32)
    counts = jnp.where(jnp.arange(TOKENS, dtype=jnp.int32) == chosen, WINDOW - 1, counts)
    return counts.astype(jnp.int32)


def plant(values, key, least, high):
    longest = values.shape.index(max(values.shape))
    spots = []
    for shift in (0, 1):
        where = [jax.random.randint(jax.random.fold_in(key, axis), (), 0, length) for axis, length in enumerate(values.shape)]
        where[longest] = (where[longest] + shift) % values.shape[longest]
        spots.append(tuple(where))
    return values.at[spots[0]].set(least).at[spots[1]].set(high)


def steps_of(stream_key, extent, cuts, smallest, top_value):
    def one(dim, parts):
        draws = jax.random.uniform(jax.random.fold_in(jax.random.fold_in(stream_key, 6), dim), (parts,), jnp.float32, smallest / len(cuts), top_value / len(cuts))
        return jnp.repeat(jnp.exp(draws), extent[dim] // parts).reshape((-1,) + (1,) * (len(extent) - dim - 1))

    loudness = one(*cuts[0])
    for cut in cuts[1:]:
        loudness = loudness * one(*cut)
    return loudness


def gaussian(key, dims, width, most, cuts=(), kind=jnp.bfloat16):
    level = steps_of(key, dims, cuts, -0.22, 0.18) if cuts else 1.0
    array = jax.random.normal(key, dims, jnp.float32) * width * level
    return jnp.minimum(jnp.maximum(array, -most), most).astype(kind)


def setup_inputs(seed: int = 0) -> dict:
    arg_keys = jax.random.split(jax.random.key(seed), 12)
    return {
        "tokens": draw_tokens(jax.random.fold_in(arg_keys[11], 71), 0),
        "attn_gain": jnp.clip(1.0 + 0.18 * jax.random.normal(arg_keys[1], (D,), jnp.float32), 0.1, 1.9),
        "w_query": gaussian(arg_keys[2], (D, D), D ** -0.5, 0.09375, ((0, 8), (1, 64))),
        "w_keyval": gaussian(arg_keys[3], (D, 2 * HD), D ** -0.5, 0.09375, ((0, 8), (1, 64))),
        "cache": draw_cache(jax.random.fold_in(arg_keys[11], 71), 0),
        "lengths": draw_lengths(jax.random.fold_in(arg_keys[11], 71), 0),
        "write_pos": plant(jax.random.randint(arg_keys[6], (TOKENS,), 0, WINDOW), jax.random.fold_in(arg_keys[6], 1), 0, WINDOW - 1).astype(jnp.int32),
        "w_out": gaussian(arg_keys[7], (D, D), D ** -0.5, 0.09375, ((0, 8), (1, 64))),
        "mlp_gain": jnp.clip(1.0 + 0.18 * jax.random.normal(arg_keys[8], (D,), jnp.float32), 0.1, 1.9),
        "w_gate_up": gaussian(arg_keys[9], (D, 2 * FF), D ** -0.5, 0.09375, ((0, 8), (1, 64))),
        "w_down": gaussian(arg_keys[10], (FF, D), FF ** -0.5, 0.0546875, ((0, 64), (1, 8))),
    }


EPSILON = 1e-06

def rms_norm(values, gain):
    wide = values.astype(jnp.float32)
    meansq = lax.optimization_barrier(jnp.mean(wide * wide, axis=-1, keepdims=True))
    return (wide * lax.rsqrt(meansq + EPSILON) * gain).astype(jnp.bfloat16)

def attend_one(inputs):
    query, key_new, value_new, keys, values, length, position = inputs
    slots = jnp.arange(WINDOW, dtype=jnp.int32)
    offset = (position - 1 - slots) % WINDOW
    usable = offset < length
    factor = 1.0 / math.sqrt(HD)
    query_wide = query.astype(jnp.float32)
    scores = jnp.einsum('he,ew->hw', query_wide, keys.astype(jnp.float32)) * factor
    scores = jnp.where(usable[None, :], scores, -jnp.inf)
    own = lax.optimization_barrier(jnp.sum(query_wide * key_new.astype(jnp.float32)[None, :], axis=-1)) * factor
    top = jnp.maximum(lax.optimization_barrier(jnp.max(scores, axis=-1)), own)
    weights = jnp.exp(scores - top[:, None])
    own_weight = jnp.exp(own - top)
    total = lax.optimization_barrier(jnp.sum(weights, axis=-1)) + own_weight
    numer = jnp.einsum('hw,ew->he', weights.astype(jnp.bfloat16).astype(jnp.float32), values.astype(jnp.float32))
    numer = numer + own_weight.astype(jnp.bfloat16).astype(jnp.float32)[:, None] * value_new.astype(jnp.float32)[None, :]
    return (numer / total[:, None]).astype(jnp.bfloat16)

def reference(tokens, attn_gain, w_query, w_keyval, cache, lengths, write_pos, w_out, mlp_gain, w_gate_up, w_down):
    chan = HD // N_CH
    ffdev = FF // N_REQ
    normed = rms_norm(tokens, attn_gain)
    query = jnp.dot(normed, w_query, preferred_element_type=jnp.float32).astype(jnp.bfloat16)
    kv_new = jnp.dot(normed, w_keyval, preferred_element_type=jnp.float32).astype(jnp.bfloat16)
    heads_query = query.reshape(TOKENS, N_CH, H, chan).transpose(0, 2, 1, 3).reshape(TOKENS, H, HD)
    split_kv = kv_new.reshape(TOKENS, N_CH, 2, chan)
    key_new = split_kv[:, :, 0, :].reshape(TOKENS, HD)
    value_new = split_kv[:, :, 1, :].reshape(TOKENS, HD)
    mixed = lax.map(attend_one, (heads_query, key_new, value_new, cache[0], cache[1], lengths, write_pos))
    attn = mixed.reshape(TOKENS, H, N_CH, chan).transpose(0, 2, 1, 3).reshape(TOKENS, D)
    first = tokens.astype(jnp.float32) + jnp.dot(attn, w_out, preferred_element_type=jnp.float32)
    first = first.astype(jnp.bfloat16)
    normed_two = rms_norm(first, mlp_gain)
    joined = jnp.dot(normed_two, w_gate_up, preferred_element_type=jnp.float32).reshape(TOKENS, N_REQ, 2, ffdev)
    gate = joined[:, :, 0, :].reshape(TOKENS, FF)
    upward = joined[:, :, 1, :].reshape(TOKENS, FF)
    hidden = (jax.nn.gelu(gate, approximate=True) * upward).astype(jnp.bfloat16)
    result = first.astype(jnp.float32) + jnp.dot(hidden, w_down, preferred_element_type=jnp.float32)
    return (result.astype(jnp.bfloat16), kv_new)
```

```python
import math

import jax
import jax.numpy as jnp
from jax import lax
from jax.sharding import PartitionSpec as P

D = 4096
H = 16
HD = 256


EPSILON = 1e-06


def gather_rows(x, axis, n):
    return lax.all_to_all(jnp.broadcast_to(x[None], (n,) + x.shape), axis, 0, 0)


def exchange(x, axis):
    return lax.all_to_all(x, axis, 0, 0)


def body(
    tokens,
    attn_gain,
    w_query,
    w_keyval,
    cache,
    lengths,
    write_pos,
    w_out,
    mlp_gain,
    w_gate_up,
    w_down,
):
    n_req = lax.axis_size("req")
    n_ch = lax.axis_size("ch")
    rows = tokens.shape[0]
    feat = tokens.shape[1]
    chan = cache.shape[2]
    window = cache.shape[3]
    total_rows = rows * n_req
    per_ch = n_req // n_ch
    factor = 1.0 / math.sqrt(HD)

    tok_all = gather_rows(tokens, "req", n_req).reshape(total_rows, feat)
    wide = tok_all.astype(jnp.float32)
    squares = jnp.sum(wide * wide, axis=1)
    scaled = (wide * attn_gain[None, :]).astype(jnp.bfloat16)
    joined = jnp.concatenate([w_query, w_keyval], axis=1)
    qcols = w_query.shape[1]
    kcols = w_keyval.shape[1]
    parts = jnp.dot(scaled, joined, preferred_element_type=jnp.float32)
    parts = jnp.concatenate([parts, squares[:, None]], axis=1)
    width = parts.shape[1]
    parts = exchange(parts.reshape(n_req, rows, width), "req")
    parts = exchange(parts.reshape(n_ch, per_ch, rows, width), "ch")
    summed = jnp.sum(parts, axis=0)
    scale = lax.rsqrt(summed[0, :, width - 1] / D + EPSILON)
    q_sum = summed[:, :, :qcols].transpose(1, 0, 2).reshape(rows, H, chan)
    kv_sum = summed[:, :, qcols:qcols + kcols].transpose(1, 0, 2).reshape(rows, 2 * chan)
    queries = (q_sum * scale[:, None, None]).astype(jnp.bfloat16)
    keyval_new = (kv_sum * scale[:, None]).astype(jnp.bfloat16)
    key_new = keyval_new[:, :chan]
    value_new = keyval_new[:, chan:]

    keys = cache[0]
    values_cache = cache[1]
    own_part = jnp.sum(
        queries.astype(jnp.float32) * key_new.astype(jnp.float32)[:, None, :], axis=-1
    )
    score_part = jnp.einsum("bhe,bew->bhw", queries, keys, preferred_element_type=jnp.float32)
    both = jnp.concatenate([score_part, own_part[..., None]], axis=-1)
    hg = H // n_ch
    both = both.reshape(rows, n_ch, hg, window + 1).transpose(1, 0, 2, 3)
    full = jnp.sum(exchange(both, "ch"), axis=0)
    scores = full[..., :window] * factor
    own_score = full[..., window] * factor
    slot_index = jnp.arange(window, dtype=jnp.int32)
    offset = (write_pos[:, None] - 1 - slot_index[None, :]) % window
    usable = offset < lengths[:, None]
    scores = jnp.where(usable[:, None, :], scores, -jnp.inf)
    top = jnp.maximum(jnp.max(scores, axis=-1), own_score)
    weights = jnp.exp(scores - top[..., None])
    own_weight = jnp.exp(own_score - top)
    total = jnp.sum(weights, axis=-1) + own_weight
    packed = jnp.concatenate([weights, own_weight[..., None], total[..., None]], axis=-1)
    back = gather_rows(packed, "ch", n_ch)
    back = back.transpose(1, 0, 2, 3).reshape(rows, H, window + 2)
    weights_low = back[..., :window].astype(jnp.bfloat16)
    own_w = back[..., window]
    tot = back[..., window + 1]
    numer = jnp.einsum(
        "bhw,bew->bhe", weights_low, values_cache, preferred_element_type=jnp.float32
    )
    numer = (
        numer
        + own_w.astype(jnp.bfloat16).astype(jnp.float32)[..., None]
        * value_new.astype(jnp.float32)[:, None, :]
    )
    attn_local = (numer / tot[..., None]).astype(jnp.bfloat16).reshape(rows, H * chan)

    attn_all = gather_rows(attn_local, "req", n_req).reshape(total_rows, H * chan)
    out_parts = jnp.dot(attn_all, w_out, preferred_element_type=jnp.float32)
    ocols = w_out.shape[1]
    out_parts = exchange(out_parts.reshape(n_req, rows, ocols), "req")
    out_parts = exchange(out_parts.reshape(n_ch, per_ch, rows, ocols), "ch")
    out_sum = jnp.sum(out_parts, axis=0).transpose(1, 0, 2).reshape(rows, per_ch * ocols)
    first = (tokens.astype(jnp.float32) + out_sum).astype(jnp.bfloat16)

    first_all = gather_rows(first, "req", n_req).reshape(total_rows, feat)
    wide2 = first_all.astype(jnp.float32)
    squares2 = jnp.sum(wide2 * wide2, axis=1)
    scaled2 = (wide2 * mlp_gain[None, :]).astype(jnp.bfloat16)
    ffn = jnp.dot(scaled2, w_gate_up, preferred_element_type=jnp.float32)
    ffn = jnp.concatenate([ffn, squares2[:, None]], axis=1)
    fw = ffn.shape[1]
    tg = total_rows // n_ch
    ffn = jnp.sum(exchange(ffn.reshape(n_ch, tg, fw), "ch"), axis=0)
    scale2 = lax.rsqrt(ffn[:, fw - 1] / D + EPSILON)
    hidden_cols = w_gate_up.shape[1] // 2
    gate = ffn[:, :hidden_cols] * scale2[:, None]
    up = ffn[:, hidden_cols:2 * hidden_cols] * scale2[:, None]
    hidden = (jax.nn.gelu(gate, approximate=True) * up).astype(jnp.bfloat16)
    hidden_all = gather_rows(hidden, "ch", n_ch).reshape(total_rows, hidden_cols)
    down = jnp.dot(hidden_all, w_down, preferred_element_type=jnp.float32)
    down = jnp.sum(exchange(down.reshape(n_req, rows, down.shape[1]), "req"), axis=0)
    layer_out = (first.astype(jnp.float32) + down).astype(jnp.bfloat16)
    return (layer_out, keyval_new)


def solution(mesh):
    placed = (
        P("req", "ch"),
        P("ch"),
        P("ch", "req"),
        P("ch", "req"),
        P(None, "req", "ch", None),
        P("req"),
        P("req"),
        P("ch", "req"),
        P("ch"),
        P("ch", "req"),
        P("req", "ch"),
    )
    return jax.shard_map(
        body,
        mesh=mesh,
        in_specs=placed,
        out_specs=(P("req", "ch"), P("req", "ch")),
        check_vma=False,
    )
```

```python
import math

import jax
import jax.numpy as jnp
from jax import lax
from jax.sharding import PartitionSpec as P

D = 4096
H = 16
HD = 256


EPSILON = 1e-06


def gather_rows(x, axis, n):
    return lax.all_to_all(jnp.broadcast_to(x[None], (n,) + x.shape), axis, 0, 0)


def exchange(x, axis):
    return lax.all_to_all(x, axis, 0, 0)


def body(
    tokens,
    attn_gain,
    w_query,
    w_keyval,
    cache,
    lengths,
    write_pos,
    w_out,
    mlp_gain,
    w_gate_up,
    w_down,
):
    n_req = lax.axis_size("req")
    n_ch = lax.axis_size("ch")
    rows = tokens.shape[0]
    feat = tokens.shape[1]
    chan = cache.shape[2]
    window = cache.shape[3]
    total_rows = rows * n_req
    per_ch = n_req // n_ch
    factor = 1.0 / math.sqrt(HD)

    tok_all = gather_rows(tokens, "req", n_req).reshape(total_rows, feat)
    wide = tok_all.astype(jnp.float32)
    squares = jnp.sum(wide * wide, axis=1)
    scaled = (wide * attn_gain[None, :]).astype(jnp.bfloat16)
    joined = jnp.concatenate([w_query, w_keyval], axis=1)
    qcols = w_query.shape[1]
    kcols = w_keyval.shape[1]
    parts = jnp.dot(scaled, joined, preferred_element_type=jnp.float32)
    parts = jnp.concatenate([parts, squares[:, None]], axis=1)
    width = parts.shape[1]
    parts = exchange(parts.reshape(n_req, rows, width), "req")
    parts = exchange(parts.reshape(n_ch, per_ch, rows, width), "ch")
    summed = jnp.sum(parts, axis=0)
    scale = lax.rsqrt(summed[0, :, width - 1] / D + EPSILON)
    q_sum = summed[:, :, :qcols].transpose(1, 0, 2).reshape(rows, H, chan)
    kv_sum = summed[:, :, qcols:qcols + kcols].transpose(1, 0, 2).reshape(rows, 2 * chan)
    queries = (q_sum * scale[:, None, None]).astype(jnp.bfloat16)
    keyval_new = (kv_sum * scale[:, None]).astype(jnp.bfloat16)
    key_new = keyval_new[:, :chan]
    value_new = keyval_new[:, chan:]

    keys = cache[0]
    values_cache = cache[1]
    own_part = jnp.sum(
        queries.astype(jnp.float32) * key_new.astype(jnp.float32)[:, None, :], axis=-1
    )
    score_part = jnp.einsum("bhe,bew->bhw", queries, keys, preferred_element_type=jnp.float32)
    both = jnp.concatenate([score_part, own_part[..., None]], axis=-1)
    hg = H // n_ch
    both = both.reshape(rows, n_ch, hg, window + 1).transpose(1, 0, 2, 3)
    full = jnp.sum(exchange(both, "ch"), axis=0)
    scores = full[..., :window] * factor
    own_score = full[..., window] * factor
    slot_index = jnp.arange(window, dtype=jnp.int32)
    offset = (write_pos[:, None] - 1 - slot_index[None, :]) % window
    usable = offset < lengths[:, None]
    scores = jnp.where(usable[:, None, :], scores, -jnp.inf)
    top = jnp.maximum(jnp.max(scores, axis=-1), own_score)
    weights = jnp.exp(scores - top[..., None])
    own_weight = jnp.exp(own_score - top)
    total = jnp.sum(weights, axis=-1) + own_weight
    total_hi = total.astype(jnp.bfloat16)
    total_lo = (total - total_hi.astype(jnp.float32)).astype(jnp.bfloat16)
    packed = jnp.concatenate(
        [
            weights.astype(jnp.bfloat16),
            own_weight.astype(jnp.bfloat16)[..., None],
            total_hi[..., None],
            total_lo[..., None],
        ],
        axis=-1,
    )
    back = gather_rows(packed, "ch", n_ch)
    back = back.transpose(1, 0, 2, 3).reshape(rows, H, window + 3)
    weights_low = back[..., :window]
    own_w = back[..., window].astype(jnp.float32)
    tot = back[..., window + 1].astype(jnp.float32) + back[..., window + 2].astype(jnp.float32)
    numer = jnp.einsum(
        "bhw,bew->bhe", weights_low, values_cache, preferred_element_type=jnp.float32
    )
    numer = (
        numer
        + own_w[..., None]
        * value_new.astype(jnp.float32)[:, None, :]
    )
    attn_local = (numer / tot[..., None]).astype(jnp.bfloat16).reshape(rows, H * chan)

    attn_all = gather_rows(attn_local, "req", n_req).reshape(total_rows, H * chan)
    out_parts = jnp.dot(attn_all, w_out, preferred_element_type=jnp.float32)
    ocols = w_out.shape[1]
    out_parts = exchange(out_parts.reshape(n_req, rows, ocols), "req")
    out_parts = exchange(out_parts.reshape(n_ch, per_ch, rows, ocols), "ch")
    out_sum = jnp.sum(out_parts, axis=0).transpose(1, 0, 2).reshape(rows, per_ch * ocols)
    first = (tokens.astype(jnp.float32) + out_sum).astype(jnp.bfloat16)

    first_all = gather_rows(first, "req", n_req).reshape(total_rows, feat)
    wide2 = first_all.astype(jnp.float32)
    squares2 = jnp.sum(wide2 * wide2, axis=1)
    scaled2 = (wide2 * mlp_gain[None, :]).astype(jnp.bfloat16)
    ffn = jnp.dot(scaled2, w_gate_up, preferred_element_type=jnp.float32)
    ffn = jnp.concatenate([ffn, squares2[:, None]], axis=1)
    fw = ffn.shape[1]
    tg = total_rows // n_ch
    ffn = jnp.sum(exchange(ffn.reshape(n_ch, tg, fw), "ch"), axis=0)
    scale2 = lax.rsqrt(ffn[:, fw - 1] / D + EPSILON)
    hidden_cols = w_gate_up.shape[1] // 2
    gate = ffn[:, :hidden_cols] * scale2[:, None]
    up = ffn[:, hidden_cols:2 * hidden_cols] * scale2[:, None]
    hidden = (jax.nn.gelu(gate, approximate=True) * up).astype(jnp.bfloat16)
    hidden_all = gather_rows(hidden, "ch", n_ch).reshape(total_rows, hidden_cols)
    down = jnp.dot(hidden_all, w_down, preferred_element_type=jnp.float32)
    down = jnp.sum(exchange(down.reshape(n_req, rows, down.shape[1]), "req"), axis=0)
    layer_out = (first.astype(jnp.float32) + down).astype(jnp.bfloat16)
    return (layer_out, keyval_new)


def solution(mesh):
    placed = (
        P("req", "ch"),
        P("ch"),
        P("ch", "req"),
        P("ch", "req"),
        P(None, "req", "ch", None),
        P("req"),
        P("req"),
        P("ch", "req"),
        P("ch"),
        P("ch", "req"),
        P("req", "ch"),
    )
    return jax.shard_map(
        body,
        mesh=mesh,
        in_specs=placed,
        out_specs=(P("req", "ch"), P("req", "ch")),
        check_vma=False,
    )
```

```python
import math

import jax
import jax.numpy as jnp
from jax import lax
from jax.sharding import PartitionSpec as P

D = 4096
H = 16
HD = 256


EPSILON = 1e-06


def gather_rows(x, axis, n):
    return lax.all_to_all(jnp.broadcast_to(x[None], (n,) + x.shape), axis, 0, 0)


def exchange(x, axis):
    return lax.all_to_all(x, axis, 0, 0)


def lane_pad(x, lanes=128):
    extra = (-x.shape[-1]) % lanes
    if extra == 0:
        return x
    return jnp.pad(x, [(0, 0)] * (x.ndim - 1) + [(0, extra)])


def body(
    tokens,
    attn_gain,
    w_query,
    w_keyval,
    cache,
    lengths,
    write_pos,
    w_out,
    mlp_gain,
    w_gate_up,
    w_down,
):
    n_req = lax.axis_size("req")
    n_ch = lax.axis_size("ch")
    rows = tokens.shape[0]
    feat = tokens.shape[1]
    chan = cache.shape[2]
    window = cache.shape[3]
    total_rows = rows * n_req
    per_ch = n_req // n_ch
    factor = 1.0 / math.sqrt(HD)

    tok_all = gather_rows(tokens.reshape(rows * feat), "req", n_req).reshape(total_rows, feat)
    wide = tok_all.astype(jnp.float32)
    squares = jnp.sum(wide * wide, axis=1)
    scaled = (wide * attn_gain[None, :]).astype(jnp.bfloat16)
    joined = jnp.concatenate([w_query, w_keyval], axis=1)
    qcols = w_query.shape[1]
    kcols = w_keyval.shape[1]
    parts = jnp.dot(scaled, joined, preferred_element_type=jnp.float32)
    parts = lane_pad(jnp.concatenate([parts, squares[:, None]], axis=1))
    width = parts.shape[1]
    sq_col = qcols + kcols
    parts = exchange(parts.reshape(n_req, rows * width), "req")
    parts = exchange(parts.reshape(n_ch, per_ch * rows * width), "ch")
    summed = jnp.sum(parts, axis=0).reshape(per_ch, rows, width)
    scale = lax.rsqrt(summed[0, :, sq_col] / D + EPSILON)
    q_sum = summed[:, :, :qcols].transpose(1, 0, 2).reshape(rows, H, chan)
    kv_sum = summed[:, :, qcols:qcols + kcols].transpose(1, 0, 2).reshape(rows, 2 * chan)
    queries = (q_sum * scale[:, None, None]).astype(jnp.bfloat16)
    keyval_new = (kv_sum * scale[:, None]).astype(jnp.bfloat16)
    key_new = keyval_new[:, :chan]
    value_new = keyval_new[:, chan:]

    keys = cache[0]
    values_cache = cache[1]
    own_part = jnp.sum(
        queries.astype(jnp.float32) * key_new.astype(jnp.float32)[:, None, :], axis=-1
    )
    score_part = jnp.einsum("bhe,bew->bhw", queries, keys, preferred_element_type=jnp.float32)
    hg = H // n_ch
    score_part = score_part.reshape(rows, n_ch, hg, window).transpose(1, 0, 2, 3)
    own_part = own_part.reshape(rows, n_ch, hg).transpose(1, 0, 2)
    both = jnp.concatenate(
        [score_part.reshape(n_ch, rows * hg * window), lane_pad(own_part.reshape(n_ch, rows * hg))],
        axis=1,
    )
    full = jnp.sum(exchange(both, "ch"), axis=0)
    scores = full[: rows * hg * window].reshape(rows, hg, window) * factor
    own_score = full[rows * hg * window: rows * hg * window + rows * hg].reshape(rows, hg) * factor
    slot_index = jnp.arange(window, dtype=jnp.int32)
    offset = (write_pos[:, None] - 1 - slot_index[None, :]) % window
    usable = offset < lengths[:, None]
    scores = jnp.where(usable[:, None, :], scores, -jnp.inf)
    top = jnp.maximum(jnp.max(scores, axis=-1), own_score)
    weights = jnp.exp(scores - top[..., None])
    own_weight = jnp.exp(own_score - top)
    total = jnp.sum(weights, axis=-1) + own_weight
    total_hi = total.astype(jnp.bfloat16)
    total_lo = (total - total_hi.astype(jnp.float32)).astype(jnp.bfloat16)
    nw = rows * hg * window
    ns = rows * hg
    stats = jnp.stack([own_weight.astype(jnp.bfloat16), total_hi, total_lo], axis=0)
    packed = jnp.concatenate(
        [weights.astype(jnp.bfloat16).reshape(nw), lane_pad(stats.reshape(3 * ns))], axis=0
    )
    back = gather_rows(packed, "ch", n_ch)
    weights_low = back[:, :nw].reshape(n_ch, rows, hg, window).transpose(1, 0, 2, 3)
    weights_low = weights_low.reshape(rows, H, window)
    stats = back[:, nw: nw + 3 * ns].astype(jnp.float32).reshape(n_ch, 3, rows, hg)
    stats = stats.transpose(1, 2, 0, 3).reshape(3, rows, H)
    own_w = stats[0]
    tot = stats[1] + stats[2]
    numer = jnp.einsum(
        "bhw,bew->bhe", weights_low, values_cache, preferred_element_type=jnp.float32
    )
    numer = (
        numer
        + own_w[..., None]
        * value_new.astype(jnp.float32)[:, None, :]
    )
    attn_local = (numer / tot[..., None]).astype(jnp.bfloat16).reshape(rows, H * chan)

    attn_all = gather_rows(attn_local.reshape(rows * H * chan), "req", n_req).reshape(total_rows, H * chan)
    out_parts = jnp.dot(attn_all, w_out, preferred_element_type=jnp.float32)
    ocols = w_out.shape[1]
    out_parts = exchange(out_parts.reshape(n_req, rows * ocols), "req")
    out_parts = exchange(out_parts.reshape(n_ch, per_ch * rows * ocols), "ch")
    out_sum = jnp.sum(out_parts, axis=0).reshape(per_ch, rows, ocols)
    out_sum = out_sum.transpose(1, 0, 2).reshape(rows, per_ch * ocols)
    first = (tokens.astype(jnp.float32) + out_sum).astype(jnp.bfloat16)

    first_all = gather_rows(first.reshape(rows * feat), "req", n_req).reshape(total_rows, feat)
    wide2 = first_all.astype(jnp.float32)
    squares2 = jnp.sum(wide2 * wide2, axis=1)
    scaled2 = (wide2 * mlp_gain[None, :]).astype(jnp.bfloat16)
    ffn = jnp.dot(scaled2, w_gate_up, preferred_element_type=jnp.float32)
    fw = ffn.shape[1]
    tg = total_rows // n_ch
    ffn = jnp.concatenate(
        [ffn.reshape(n_ch, tg * fw), lane_pad(squares2.reshape(n_ch, tg))], axis=1
    )
    ffn = jnp.sum(exchange(ffn, "ch"), axis=0)
    scale2 = lax.rsqrt(ffn[tg * fw: tg * fw + tg] / D + EPSILON)
    ffn = ffn[: tg * fw].reshape(tg, fw)
    hidden_cols = w_gate_up.shape[1] // 2
    gate = ffn[:, :hidden_cols] * scale2[:, None]
    up = ffn[:, hidden_cols:2 * hidden_cols] * scale2[:, None]
    hidden = (jax.nn.gelu(gate, approximate=True) * up).astype(jnp.bfloat16)
    hidden_all = gather_rows(hidden.reshape(tg * hidden_cols), "ch", n_ch).reshape(total_rows, hidden_cols)
    down = jnp.dot(hidden_all, w_down, preferred_element_type=jnp.float32)
    dcols = down.shape[1]
    down = jnp.sum(exchange(down.reshape(n_req, rows * dcols), "req"), axis=0).reshape(rows, dcols)
    layer_out = (first.astype(jnp.float32) + down).astype(jnp.bfloat16)
    return (layer_out, keyval_new)


def solution(mesh):
    placed = (
        P("req", "ch"),
        P("ch"),
        P("ch", "req"),
        P("ch", "req"),
        P(None, "req", "ch", None),
        P("req"),
        P("req"),
        P("ch", "req"),
        P("ch"),
        P("ch", "req"),
        P("req", "ch"),
    )
    return jax.shard_map(
        body,
        mesh=mesh,
        in_specs=placed,
        out_specs=(P("req", "ch"), P("req", "ch")),
        check_vma=False,
    )
```

```python
import math

import jax
import jax.numpy as jnp
from jax import lax
from jax.sharding import PartitionSpec as P

D = 4096
H = 16
HD = 256


EPSILON = 1e-06


def gather_rows(x, axis, n):
    return lax.all_to_all(jnp.broadcast_to(x[None], (n,) + x.shape), axis, 0, 0)


def exchange(x, axis):
    return lax.all_to_all(x, axis, 0, 0)


def body(
    tokens,
    attn_gain,
    w_query,
    w_keyval,
    cache,
    lengths,
    write_pos,
    w_out,
    mlp_gain,
    w_gate_up,
    w_down,
):
    n_req = lax.axis_size("req")
    n_ch = lax.axis_size("ch")
    rows = tokens.shape[0]
    feat = tokens.shape[1]
    chan = cache.shape[2]
    window = cache.shape[3]
    total_rows = rows * n_req
    per_ch = n_req // n_ch
    factor = 1.0 / math.sqrt(HD)

    tok_all = gather_rows(tokens, "req", n_req).reshape(total_rows, feat)
    wide = tok_all.astype(jnp.float32)
    squares = jnp.sum(wide * wide, axis=1)
    scaled = (wide * attn_gain[None, :]).astype(jnp.bfloat16)
    joined = jnp.concatenate([w_query, w_keyval], axis=1)
    qcols = w_query.shape[1]
    kcols = w_keyval.shape[1]
    parts = jnp.dot(scaled, joined, preferred_element_type=jnp.float32)
    parts = jnp.concatenate([parts, squares[:, None]], axis=1)
    width = parts.shape[1]
    parts = exchange(parts.reshape(n_req, rows, width), "req")
    parts = exchange(parts.reshape(n_ch, per_ch, rows, width), "ch")
    summed = jnp.sum(parts, axis=0)
    scale = lax.rsqrt(summed[0, :, width - 1] / D + EPSILON)
    q_sum = summed[:, :, :qcols].transpose(1, 0, 2).reshape(rows, H, chan)
    kv_sum = summed[:, :, qcols:qcols + kcols].transpose(1, 0, 2).reshape(rows, 2 * chan)
    queries = (q_sum * scale[:, None, None]).astype(jnp.bfloat16)
    keyval_new = (kv_sum * scale[:, None]).astype(jnp.bfloat16)
    key_new = keyval_new[:, :chan]
    value_new = keyval_new[:, chan:]

    keys = cache[0]
    values_cache = cache[1]
    own_part = jnp.sum(
        queries.astype(jnp.float32) * key_new.astype(jnp.float32)[:, None, :], axis=-1
    )
    score_part = jnp.einsum("bhe,bew->bhw", queries, keys, preferred_element_type=jnp.float32)
    both = jnp.concatenate([score_part, own_part[..., None]], axis=-1)
    hg = H // n_ch
    both = both.reshape(rows, n_ch, hg, window + 1).transpose(1, 0, 2, 3)
    full = jnp.sum(exchange(both, "ch"), axis=0)
    scores = full[..., :window] * factor
    own_score = full[..., window] * factor
    slot_index = jnp.arange(window, dtype=jnp.int32)
    offset = (write_pos[:, None] - 1 - slot_index[None, :]) % window
    usable = offset < lengths[:, None]
    scores = jnp.where(usable[:, None, :], scores, -jnp.inf)
    top = jnp.maximum(jnp.max(scores, axis=-1), own_score)
    weights = jnp.exp(scores - top[..., None])
    own_weight = jnp.exp(own_score - top)
    total = jnp.sum(weights, axis=-1) + own_weight
    total_hi = total.astype(jnp.bfloat16)
    total_lo = (total - total_hi.astype(jnp.float32)).astype(jnp.bfloat16)
    packed = jnp.concatenate(
        [
            weights.astype(jnp.bfloat16),
            own_weight.astype(jnp.bfloat16)[..., None],
            total_hi[..., None],
            total_lo[..., None],
        ],
        axis=-1,
    )
    back = gather_rows(packed, "ch", n_ch)
    back = back.transpose(1, 0, 2, 3).reshape(rows, H, window + 3)
    weights_low = back[..., :window]
    own_w = back[..., window].astype(jnp.float32)
    tot = back[..., window + 1].astype(jnp.float32) + back[..., window + 2].astype(jnp.float32)
    numer = jnp.einsum(
        "bhw,bew->bhe", weights_low, values_cache, preferred_element_type=jnp.float32
    )
    numer = (
        numer
        + own_w[..., None]
        * value_new.astype(jnp.float32)[:, None, :]
    )
    attn_local = (numer / tot[..., None]).astype(jnp.bfloat16).reshape(rows, H * chan)

    attn_all = gather_rows(attn_local, "req", n_req).reshape(total_rows, H * chan)
    out_parts = jnp.dot(attn_all, w_out, preferred_element_type=jnp.float32)
    ocols = w_out.shape[1]
    out_parts = exchange(out_parts.reshape(n_req, rows, ocols), "req")
    out_parts = exchange(out_parts.reshape(n_ch, per_ch, rows, ocols), "ch")
    out_sum = jnp.sum(out_parts, axis=0).transpose(1, 0, 2).reshape(rows, per_ch * ocols)
    first = (tokens.astype(jnp.float32) + out_sum).astype(jnp.bfloat16)

    first_all = gather_rows(first, "req", n_req).reshape(total_rows, feat)
    wide2 = first_all.astype(jnp.float32)
    squares2 = jnp.sum(wide2 * wide2, axis=1)
    scaled2 = (wide2 * mlp_gain[None, :]).astype(jnp.bfloat16)
    ffn = jnp.dot(scaled2, w_gate_up, preferred_element_type=jnp.float32)
    sq_hi = squares2.astype(jnp.bfloat16)
    sq_lo = (squares2 - sq_hi.astype(jnp.float32)).astype(jnp.bfloat16)
    ffn = jnp.concatenate([ffn.astype(jnp.bfloat16), sq_hi[:, None], sq_lo[:, None]], axis=1)
    fw = ffn.shape[1]
    tg = total_rows // n_ch
    ffn = exchange(ffn.reshape(n_ch, tg, fw), "ch")
    ffn = jnp.sum(ffn.astype(jnp.float32), axis=0)
    scale2 = lax.rsqrt((ffn[:, fw - 2] + ffn[:, fw - 1]) / D + EPSILON)
    hidden_cols = w_gate_up.shape[1] // 2
    gate = ffn[:, :hidden_cols] * scale2[:, None]
    up = ffn[:, hidden_cols:2 * hidden_cols] * scale2[:, None]
    hidden = (jax.nn.gelu(gate, approximate=True) * up).astype(jnp.bfloat16)
    hidden_all = gather_rows(hidden, "ch", n_ch).reshape(total_rows, hidden_cols)
    down = jnp.dot(hidden_all, w_down, preferred_element_type=jnp.float32)
    down = exchange(down.astype(jnp.bfloat16).reshape(n_req, rows, down.shape[1]), "req")
    down = jnp.sum(down.astype(jnp.float32), axis=0)
    layer_out = (first.astype(jnp.float32) + down).astype(jnp.bfloat16)
    return (layer_out, keyval_new)


def solution(mesh):
    placed = (
        P("req", "ch"),
        P("ch"),
        P("ch", "req"),
        P("ch", "req"),
        P(None, "req", "ch", None),
        P("req"),
        P("req"),
        P("ch", "req"),
        P("ch"),
        P("ch", "req"),
        P("req", "ch"),
    )
    return jax.shard_map(
        body,
        mesh=mesh,
        in_specs=placed,
        out_specs=(P("req", "ch"), P("req", "ch")),
        check_vma=False,
    )
```

```python
import math

import jax
import jax.numpy as jnp
from jax import lax
from jax.sharding import PartitionSpec as P

D = 4096
H = 16
HD = 256


EPSILON = 1e-06


def gather_rows(x, axis, n):
    return lax.all_to_all(jnp.broadcast_to(x[None], (n,) + x.shape), axis, 0, 0)


def exchange(x, axis):
    return lax.all_to_all(x, axis, 0, 0)


def body(
    tokens,
    attn_gain,
    w_query,
    w_keyval,
    cache,
    lengths,
    write_pos,
    w_out,
    mlp_gain,
    w_gate_up,
    w_down,
):
    n_req = lax.axis_size("req")
    n_ch = lax.axis_size("ch")
    rows = tokens.shape[0]
    feat = tokens.shape[1]
    chan = cache.shape[2]
    window = cache.shape[3]
    total_rows = rows * n_req
    per_ch = n_req // n_ch
    factor = 1.0 / math.sqrt(HD)

    tok_all = gather_rows(tokens, "req", n_req).reshape(total_rows, feat)
    wide = tok_all.astype(jnp.float32)
    squares = jnp.sum(wide * wide, axis=1)
    scaled = (wide * attn_gain[None, :]).astype(jnp.bfloat16)
    joined = jnp.concatenate([w_query, w_keyval], axis=1)
    qcols = w_query.shape[1]
    kcols = w_keyval.shape[1]
    parts = jnp.dot(scaled, joined, preferred_element_type=jnp.float32)
    parts = jnp.concatenate([parts, squares[:, None]], axis=1)
    width = parts.shape[1]
    parts = exchange(parts.reshape(n_req, rows, width), "req")
    parts = exchange(parts.reshape(n_ch, per_ch, rows, width), "ch")
    summed = jnp.sum(parts, axis=0)
    scale = lax.rsqrt(summed[0, :, width - 1] / D + EPSILON)
    q_sum = summed[:, :, :qcols].transpose(1, 0, 2).reshape(rows, H, chan)
    kv_sum = summed[:, :, qcols:qcols + kcols].transpose(1, 0, 2).reshape(rows, 2 * chan)
    queries = (q_sum * scale[:, None, None]).astype(jnp.bfloat16)
    keyval_new = (kv_sum * scale[:, None]).astype(jnp.bfloat16)
    key_new = keyval_new[:, :chan]
    value_new = keyval_new[:, chan:]

    keys = cache[0]
    values_cache = cache[1]
    own_part = jnp.sum(
        queries.astype(jnp.float32) * key_new.astype(jnp.float32)[:, None, :], axis=-1
    )
    score_part = jnp.einsum("bhe,bew->bhw", queries, keys, preferred_element_type=jnp.float32)
    both = jnp.concatenate([score_part, own_part[..., None]], axis=-1)
    hg = H // n_ch
    both = both.reshape(rows, n_ch, hg, window + 1).transpose(1, 0, 2, 3)
    full = jnp.sum(exchange(both, "ch"), axis=0)
    scores = full[..., :window] * factor
    own_score = full[..., window] * factor
    slot_index = jnp.arange(window, dtype=jnp.int32)
    offset = (write_pos[:, None] - 1 - slot_index[None, :]) % window
    usable = offset < lengths[:, None]
    scores = jnp.where(usable[:, None, :], scores, -jnp.inf)
    top = jnp.maximum(jnp.max(scores, axis=-1), own_score)
    weights = jnp.exp(scores - top[..., None])
    own_weight = jnp.exp(own_score - top)
    total = jnp.sum(weights, axis=-1) + own_weight
    total_hi = total.astype(jnp.bfloat16)
    total_lo = (total - total_hi.astype(jnp.float32)).astype(jnp.bfloat16)
    packed = jnp.concatenate(
        [
            weights.astype(jnp.bfloat16),
            own_weight.astype(jnp.bfloat16)[..., None],
            total_hi[..., None],
            total_lo[..., None],
        ],
        axis=-1,
    )
    back = gather_rows(packed, "ch", n_ch)
    back = back.transpose(1, 0, 2, 3).reshape(rows, H, window + 3)
    weights_low = back[..., :window]
    own_w = back[..., window].astype(jnp.float32)
    tot = back[..., window + 1].astype(jnp.float32) + back[..., window + 2].astype(jnp.float32)
    numer = jnp.einsum(
        "bhw,bew->bhe", weights_low, values_cache, preferred_element_type=jnp.float32
    )
    numer = (
        numer
        + own_w[..., None]
        * value_new.astype(jnp.float32)[:, None, :]
    )
    attn_local = (numer / tot[..., None]).astype(jnp.bfloat16).reshape(rows, H * chan)

    attn_all = gather_rows(attn_local, "req", n_req).reshape(total_rows, H * chan)
    ocols = w_out.shape[1]
    lanes = max(ocols, 128)
    w_out_wide = jnp.pad(w_out, ((0, 0), (0, lanes - ocols)))
    out_parts = jnp.dot(attn_all, w_out_wide, preferred_element_type=jnp.float32)
    out_parts = exchange(out_parts.reshape(n_req, rows, lanes), "req")
    out_parts = exchange(out_parts.reshape(n_ch, per_ch, rows, lanes), "ch")
    out_sum = jnp.sum(out_parts, axis=0)[..., :ocols]
    out_sum = out_sum.transpose(1, 0, 2).reshape(rows, per_ch * ocols)
    first = (tokens.astype(jnp.float32) + out_sum).astype(jnp.bfloat16)

    first_all = gather_rows(first, "req", n_req).reshape(total_rows, feat)
    wide2 = first_all.astype(jnp.float32)
    squares2 = jnp.sum(wide2 * wide2, axis=1)
    scaled2 = (wide2 * mlp_gain[None, :]).astype(jnp.bfloat16)
    ffn = jnp.dot(scaled2, w_gate_up, preferred_element_type=jnp.float32)
    sq_hi = squares2.astype(jnp.bfloat16)
    sq_lo = (squares2 - sq_hi.astype(jnp.float32)).astype(jnp.bfloat16)
    ffn = jnp.concatenate([ffn.astype(jnp.bfloat16), sq_hi[:, None], sq_lo[:, None]], axis=1)
    fw = ffn.shape[1]
    tg = total_rows // n_ch
    ffn = exchange(ffn.reshape(n_ch, tg, fw), "ch")
    ffn = jnp.sum(ffn.astype(jnp.float32), axis=0)
    scale2 = lax.rsqrt((ffn[:, fw - 2] + ffn[:, fw - 1]) / D + EPSILON)
    hidden_cols = w_gate_up.shape[1] // 2
    gate = ffn[:, :hidden_cols] * scale2[:, None]
    up = ffn[:, hidden_cols:2 * hidden_cols] * scale2[:, None]
    hidden = (jax.nn.gelu(gate, approximate=True) * up).astype(jnp.bfloat16)
    hidden_all = gather_rows(hidden, "ch", n_ch).reshape(total_rows, hidden_cols)
    down = jnp.dot(hidden_all, w_down, preferred_element_type=jnp.float32)
    down = exchange(down.astype(jnp.bfloat16).reshape(n_req, rows, down.shape[1]), "req")
    down = jnp.sum(down.astype(jnp.float32), axis=0)
    layer_out = (first.astype(jnp.float32) + down).astype(jnp.bfloat16)
    return (layer_out, keyval_new)


def solution(mesh):
    placed = (
        P("req", "ch"),
        P("ch"),
        P("ch", "req"),
        P("ch", "req"),
        P(None, "req", "ch", None),
        P("req"),
        P("req"),
        P("ch", "req"),
        P("ch"),
        P("ch", "req"),
        P("req", "ch"),
    )
    return jax.shard_map(
        body,
        mesh=mesh,
        in_specs=placed,
        out_specs=(P("req", "ch"), P("req", "ch")),
        check_vma=False,
    )
```

```python
import math

import jax
import jax.numpy as jnp
from jax import lax
from jax.sharding import PartitionSpec as P

D = 4096
H = 16
HD = 256


EPSILON = 1e-06


def gather_rows(x, axis, n):
    return lax.all_to_all(jnp.broadcast_to(x[None], (n,) + x.shape), axis, 0, 0)


def exchange(x, axis):
    return lax.all_to_all(x, axis, 0, 0)


def body(
    tokens,
    attn_gain,
    w_query,
    w_keyval,
    cache,
    lengths,
    write_pos,
    w_out,
    mlp_gain,
    w_gate_up,
    w_down,
):
    n_req = lax.axis_size("req")
    n_ch = lax.axis_size("ch")
    rows = tokens.shape[0]
    feat = tokens.shape[1]
    chan = cache.shape[2]
    window = cache.shape[3]
    total_rows = rows * n_req
    per_ch = n_req // n_ch
    factor = 1.0 / math.sqrt(HD)

    slot_index = jnp.arange(window, dtype=jnp.int32)
    offset = (write_pos[:, None] - 1 - slot_index[None, :]) % window
    usable = offset < lengths[:, None]
    tok_bcast = jnp.broadcast_to(tokens[None], (n_req,) + tokens.shape)
    tok_bcast, usable = lax.optimization_barrier((tok_bcast, usable))
    tokens_wide = tok_bcast[0].astype(jnp.float32)

    tok_all = exchange(tok_bcast, "req").reshape(total_rows, feat)
    wide = tok_all.astype(jnp.float32)
    squares = jnp.sum(wide * wide, axis=1)
    scaled = (wide * attn_gain[None, :]).astype(jnp.bfloat16)
    joined = jnp.concatenate([w_query, w_keyval], axis=1)
    qcols = w_query.shape[1]
    kcols = w_keyval.shape[1]
    parts = jnp.dot(scaled, joined, preferred_element_type=jnp.float32)
    parts = jnp.concatenate([parts, squares[:, None]], axis=1)
    width = parts.shape[1]
    parts = exchange(parts.reshape(n_req, rows, width), "req")
    parts = exchange(parts.reshape(n_ch, per_ch, rows, width), "ch")
    summed = jnp.sum(parts, axis=0)
    scale = lax.rsqrt(summed[0, :, width - 1] / D + EPSILON)
    q_sum = summed[:, :, :qcols].transpose(1, 0, 2).reshape(rows, H, chan)
    kv_sum = summed[:, :, qcols:qcols + kcols].transpose(1, 0, 2).reshape(rows, 2 * chan)
    queries = (q_sum * scale[:, None, None]).astype(jnp.bfloat16)
    keyval_new = (kv_sum * scale[:, None]).astype(jnp.bfloat16)
    key_new = keyval_new[:, :chan]
    value_new = keyval_new[:, chan:]

    keys = cache[0]
    values_cache = cache[1]
    own_part = jnp.sum(
        queries.astype(jnp.float32) * key_new.astype(jnp.float32)[:, None, :], axis=-1
    )
    score_part = jnp.einsum("bhe,bew->bhw", queries, keys, preferred_element_type=jnp.float32)
    both = jnp.concatenate([score_part, own_part[..., None]], axis=-1)
    hg = H // n_ch
    both = both.reshape(rows, n_ch, hg, window + 1).transpose(1, 0, 2, 3)
    full = jnp.sum(exchange(both, "ch"), axis=0)
    scores = full[..., :window] * factor
    own_score = full[..., window] * factor
    scores = jnp.where(usable[:, None, :], scores, -jnp.inf)
    top = jnp.maximum(jnp.max(scores, axis=-1), own_score)
    weights = jnp.exp(scores - top[..., None])
    own_weight = jnp.exp(own_score - top)
    total = jnp.sum(weights, axis=-1) + own_weight
    total_hi = total.astype(jnp.bfloat16)
    total_lo = (total - total_hi.astype(jnp.float32)).astype(jnp.bfloat16)
    packed = jnp.concatenate(
        [
            weights.astype(jnp.bfloat16),
            own_weight.astype(jnp.bfloat16)[..., None],
            total_hi[..., None],
            total_lo[..., None],
        ],
        axis=-1,
    )
    back = gather_rows(packed, "ch", n_ch)
    back = back.transpose(1, 0, 2, 3).reshape(rows, H, window + 3)
    weights_low = back[..., :window]
    own_w = back[..., window].astype(jnp.float32)
    tot = back[..., window + 1].astype(jnp.float32) + back[..., window + 2].astype(jnp.float32)
    numer = jnp.einsum(
        "bhw,bew->bhe", weights_low, values_cache, preferred_element_type=jnp.float32
    )
    numer = (
        numer
        + own_w[..., None]
        * value_new.astype(jnp.float32)[:, None, :]
    )
    attn_local = (numer / tot[..., None]).astype(jnp.bfloat16).reshape(rows, H * chan)

    attn_all = gather_rows(attn_local, "req", n_req).reshape(total_rows, H * chan)
    ocols = w_out.shape[1]
    lanes = max(ocols, 128)
    out_parts = jnp.dot(attn_all, w_out, preferred_element_type=jnp.float32)
    out_parts = jnp.pad(out_parts, ((0, 0), (0, lanes - ocols)))
    out_parts = exchange(out_parts.reshape(n_req, rows, lanes), "req")
    out_parts = exchange(out_parts.reshape(n_ch, per_ch, rows, lanes), "ch")
    out_sum = jnp.sum(out_parts, axis=0)[..., :ocols]
    out_sum = out_sum.transpose(1, 0, 2).reshape(rows, per_ch * ocols)
    first = (tokens_wide + out_sum).astype(jnp.bfloat16)

    first_all = gather_rows(first, "req", n_req).reshape(total_rows, feat)
    wide2 = first_all.astype(jnp.float32)
    squares2 = jnp.sum(wide2 * wide2, axis=1)
    scaled2 = (wide2 * mlp_gain[None, :]).astype(jnp.bfloat16)
    ffn = jnp.dot(scaled2, w_gate_up, preferred_element_type=jnp.float32)
    sq_hi = squares2.astype(jnp.bfloat16)
    sq_lo = (squares2 - sq_hi.astype(jnp.float32)).astype(jnp.bfloat16)
    ffn = jnp.concatenate([ffn.astype(jnp.bfloat16), sq_hi[:, None], sq_lo[:, None]], axis=1)
    fw = ffn.shape[1]
    tg = total_rows // n_ch
    ffn = exchange(ffn.reshape(n_ch, tg, fw), "ch")
    ffn = jnp.sum(ffn.astype(jnp.float32), axis=0)
    scale2 = lax.rsqrt((ffn[:, fw - 2] + ffn[:, fw - 1]) / D + EPSILON)
    hidden_cols = w_gate_up.shape[1] // 2
    gate = ffn[:, :hidden_cols] * scale2[:, None]
    up = ffn[:, hidden_cols:2 * hidden_cols] * scale2[:, None]
    hidden = (jax.nn.gelu(gate, approximate=True) * up).astype(jnp.bfloat16)
    hidden_all = gather_rows(hidden, "ch", n_ch).reshape(total_rows, hidden_cols)
    down = jnp.dot(hidden_all, w_down, preferred_element_type=jnp.float32)
    down_payload = down.astype(jnp.bfloat16).reshape(n_req, rows, down.shape[1])
    down_payload, first_wide = lax.optimization_barrier((down_payload, first.astype(jnp.float32)))
    down = jnp.sum(exchange(down_payload, "req").astype(jnp.float32), axis=0)
    layer_out = (first_wide + down).astype(jnp.bfloat16)
    layer_out, keyval_out = lax.optimization_barrier((layer_out, keyval_new))
    return (layer_out, keyval_out)


def solution(mesh):
    placed = (
        P("req", "ch"),
        P("ch"),
        P("ch", "req"),
        P("ch", "req"),
        P(None, "req", "ch", None),
        P("req"),
        P("req"),
        P("ch", "req"),
        P("ch"),
        P("ch", "req"),
        P("req", "ch"),
    )
    return jax.shard_map(
        body,
        mesh=mesh,
        in_specs=placed,
        out_specs=(P("req", "ch"), P("req", "ch")),
        check_vma=False,
    )
```

```python
import math

import jax
import jax.numpy as jnp
from jax import lax
from jax.sharding import PartitionSpec as P

D = 4096
H = 16
HD = 256


EPSILON = 1e-06


def gather_rows(x, axis, n):
    return lax.all_to_all(jnp.broadcast_to(x[None], (n,) + x.shape), axis, 0, 0)


def exchange(x, axis):
    return lax.all_to_all(x, axis, 0, 0)


def body(
    tokens,
    attn_gain,
    w_query,
    w_keyval,
    cache,
    lengths,
    write_pos,
    w_out,
    mlp_gain,
    w_gate_up,
    w_down,
):
    n_req = lax.axis_size("req")
    n_ch = lax.axis_size("ch")
    rows = tokens.shape[0]
    feat = tokens.shape[1]
    chan = cache.shape[2]
    window = cache.shape[3]
    total_rows = rows * n_req
    per_ch = n_req // n_ch
    factor = 1.0 / math.sqrt(HD)

    slot_index = jnp.arange(window, dtype=jnp.int32)
    offset = (write_pos[:, None] - 1 - slot_index[None, :]) % window
    usable = offset < lengths[:, None]
    tok_bcast = jnp.broadcast_to(tokens[None], (n_req,) + tokens.shape)
    tok_bcast, usable = lax.optimization_barrier((tok_bcast, usable))
    tokens_wide = tok_bcast[0].astype(jnp.float32)

    tok_all = exchange(tok_bcast, "req").reshape(total_rows, feat)
    wide = tok_all.astype(jnp.float32)
    squares = jnp.sum(wide * wide, axis=1)
    scaled = (wide * attn_gain[None, :]).astype(jnp.bfloat16)
    qcols = w_query.shape[1]
    kcols = w_keyval.shape[1]
    spare = jnp.zeros((w_query.shape[0], 1), w_query.dtype)
    joined = jnp.concatenate([w_query, w_keyval, spare], axis=1)
    parts = jnp.dot(scaled, joined, preferred_element_type=jnp.float32)
    width = parts.shape[1]
    is_sq = jnp.arange(width, dtype=jnp.int32)[None, :] == width - 1
    parts = jnp.where(is_sq, squares[:, None], parts)
    parts = exchange(parts.reshape(n_req, rows, width), "req")
    parts = exchange(parts.reshape(n_ch, per_ch, rows, width), "ch")
    summed = jnp.sum(parts, axis=0)
    scale = lax.rsqrt(summed[0, :, width - 1] / D + EPSILON)
    q_sum = summed[:, :, :qcols].transpose(1, 0, 2).reshape(rows, H, chan)
    kv_sum = summed[:, :, qcols:qcols + kcols].transpose(1, 0, 2).reshape(rows, 2 * chan)
    queries = (q_sum * scale[:, None, None]).astype(jnp.bfloat16)
    keyval_new = (kv_sum * scale[:, None]).astype(jnp.bfloat16)
    key_new = keyval_new[:, :chan]
    value_new = keyval_new[:, chan:]

    keys = cache[0]
    values_cache = cache[1]
    own_part = jnp.sum(
        queries.astype(jnp.float32) * key_new.astype(jnp.float32)[:, None, :], axis=-1
    )
    score_part = jnp.einsum("bhe,bew->bhw", queries, keys, preferred_element_type=jnp.float32)
    both = jnp.concatenate([score_part, own_part[..., None]], axis=-1)
    hg = H // n_ch
    both = both.reshape(rows, n_ch, hg, window + 1).transpose(1, 0, 2, 3)
    full = jnp.sum(exchange(both, "ch"), axis=0)
    scores = full[..., :window] * factor
    own_score = full[..., window] * factor
    scores = jnp.where(usable[:, None, :], scores, -jnp.inf)
    top = jnp.maximum(jnp.max(scores, axis=-1), own_score)
    weights = jnp.exp(scores - top[..., None])
    own_weight = jnp.exp(own_score - top)
    total = jnp.sum(weights, axis=-1) + own_weight
    total_hi = total.astype(jnp.bfloat16)
    total_lo = (total - total_hi.astype(jnp.float32)).astype(jnp.bfloat16)
    packed = jnp.concatenate(
        [
            weights.astype(jnp.bfloat16),
            own_weight.astype(jnp.bfloat16)[..., None],
            total_hi[..., None],
            total_lo[..., None],
        ],
        axis=-1,
    )
    back = gather_rows(packed, "ch", n_ch)
    back = back.transpose(1, 0, 2, 3).reshape(rows, H, window + 3)
    weights_low = back[..., :window]
    own_w = back[..., window].astype(jnp.float32)
    tot = back[..., window + 1].astype(jnp.float32) + back[..., window + 2].astype(jnp.float32)
    numer = jnp.einsum(
        "bhw,bew->bhe", weights_low, values_cache, preferred_element_type=jnp.float32
    )
    numer = (
        numer
        + own_w[..., None]
        * value_new.astype(jnp.float32)[:, None, :]
    )
    attn_local = (numer / tot[..., None]).astype(jnp.bfloat16).reshape(rows, H * chan)

    attn_all = gather_rows(attn_local, "req", n_req).reshape(total_rows, H * chan)
    ocols = w_out.shape[1]
    lanes = max(ocols, 128)
    out_parts = jnp.dot(attn_all, w_out, preferred_element_type=jnp.float32)
    out_parts = jnp.pad(out_parts, ((0, 0), (0, lanes - ocols)))
    out_parts = exchange(out_parts.reshape(n_req, rows, lanes), "req")
    out_parts = exchange(out_parts.reshape(n_ch, per_ch, rows, lanes), "ch")
    out_sum = jnp.sum(out_parts, axis=0)[..., :ocols]
    out_sum = out_sum.transpose(1, 0, 2).reshape(rows, per_ch * ocols)
    first = (tokens_wide + out_sum).astype(jnp.bfloat16)

    first_all = gather_rows(first, "req", n_req).reshape(total_rows, feat)
    wide2 = first_all.astype(jnp.float32)
    squares2 = jnp.sum(wide2 * wide2, axis=1)
    scaled2 = (wide2 * mlp_gain[None, :]).astype(jnp.bfloat16)
    ffn = jnp.dot(scaled2, w_gate_up, preferred_element_type=jnp.float32)
    sq_hi = squares2.astype(jnp.bfloat16)
    sq_lo = (squares2 - sq_hi.astype(jnp.float32)).astype(jnp.bfloat16)
    ffn = jnp.concatenate([ffn.astype(jnp.bfloat16), sq_hi[:, None], sq_lo[:, None]], axis=1)
    fw = ffn.shape[1]
    tg = total_rows // n_ch
    ffn = exchange(ffn.reshape(n_ch, tg, fw), "ch")
    ffn = jnp.sum(ffn.astype(jnp.float32), axis=0)
    scale2 = lax.rsqrt((ffn[:, fw - 2] + ffn[:, fw - 1]) / D + EPSILON)
    hidden_cols = w_gate_up.shape[1] // 2
    gate = ffn[:, :hidden_cols] * scale2[:, None]
    up = ffn[:, hidden_cols:2 * hidden_cols] * scale2[:, None]
    hidden = (jax.nn.gelu(gate, approximate=True) * up).astype(jnp.bfloat16)
    hidden_all = gather_rows(hidden, "ch", n_ch).reshape(total_rows, hidden_cols)
    down = jnp.dot(hidden_all, w_down, preferred_element_type=jnp.float32)
    down = exchange(down.astype(jnp.bfloat16).reshape(n_req, rows, down.shape[1]), "req")
    down = jnp.sum(down.astype(jnp.float32), axis=0)
    layer_out = (first.astype(jnp.float32) + down).astype(jnp.bfloat16)
    return (layer_out, keyval_new)


def solution(mesh):
    placed = (
        P("req", "ch"),
        P("ch"),
        P("ch", "req"),
        P("ch", "req"),
        P(None, "req", "ch", None),
        P("req"),
        P("req"),
        P("ch", "req"),
        P("ch"),
        P("ch", "req"),
        P("req", "ch"),
    )
    return jax.shard_map(
        body,
        mesh=mesh,
        in_specs=placed,
        out_specs=(P("req", "ch"), P("req", "ch")),
        check_vma=False,
    )
```
